1024 devices in a mesh: dp: 128 (over z, y_hi, core), fsdp: 8 (over y_lo, x).
Axes of the slice: x: 4, y: 8 (y_hi: 4, y_lo: 2; y = y_hi * 2 + y_lo), z: 16, core: 2. Of those that a mesh axis runs over, the one named last changes fastest.
Arguments:
- tokens: bfloat16 [16384, 3072], P('dp', 'fsdp'), may hold values from -6 to 6
- weight_blocks: bfloat16 [96, 3, 128, 128], P('fsdp'), may hold values from -0.3125 to 0.3125
- pattern: int32 [96, 3], P('fsdp'), may hold values from 0 to 23, as said below
- grad_out: bfloat16 [16384, 12288], P('dp', 'fsdp'), may hold values from -6 to 6
Outputs:
- projected: bfloat16 [16384, 12288], P('dp', 'fsdp')
- grad_tokens: bfloat16 [16384, 3072], P('dp', 'fsdp')
- grad_weight: float32 [96, 3, 16384], P('fsdp', None, 'dp')
The draws below stay inside these ranges and needn't reach their ends.
Inputs may be any that keep to these rules, and one draw needn't show every extreme that they name: `pattern`: each block-column names 3 different block-rows; every block-row is named by exactly 12 block-columns.
All inputs are finite; a program needn't handle non-finite values.
Results may differ from the reference program's by a relative error of at most 0.001.
Values may be sent and summed in bfloat16 or wider, within the bound.
No kernel may reach another device: no remote copies, remote signals or barrier semaphores. Data moves between devices by JAX's collectives and lax.ppermute only.
A program may use at most 32 MiB of HBM per device.

```python
import jax
import jax.numpy as jnp
from jax import lax

D = 3072
F = 12288
BLK = 128
K = 3
RB = 24
FB = 96
TOKENS = 16384


def draw_pattern(key, part):
    first_key, second_key = jax.random.split(jax.random.fold_in(key, 7))
    order = jax.random.permutation(first_key, RB)
    offset = jax.random.randint(second_key, (), 0, RB)
    base = (jnp.arange(FB, dtype=jnp.int32) + offset) % RB
    slots = jnp.arange(K, dtype=jnp.int32)
    rows = order[jnp.bitwise_xor(base[:, None], slots[None, :])]
    return rows.astype(jnp.int32)


def level_of(key, dims, cuts, low, largest):
    loudness, own = 1.0, jax.random.fold_in(key, 6)
    for dim, shards_of in cuts:
        draws = jnp.exp(jax.random.uniform(jax.random.fold_in(own, dim), (shards_of,), jnp.float32, low / len(cuts), largest / len(cuts)))
        loudness = loudness * jnp.repeat(draws, dims[dim] // shards_of).reshape([-1 if axis == dim else 1 for axis in range(len(dims))])
    return loudness


def gaussian(own_key, shape, width, most, shards=(), kind=jnp.bfloat16):
    entries = jax.random.normal(own_key, shape, jnp.float32) * width
    if len(shards) > 0:
        entries = level_of(own_key, shape, shards, -0.22, 0.18) * entries
    return jnp.clip(entries, min=-most, max=most).astype(kind)


def setup_inputs(seed: int = 0) -> dict:
    key_of = jax.random.split(jax.random.key(seed), 5)
    return {
        "tokens": gaussian(key_of[0], (TOKENS, D), 1.0, 6.0, ((0, 128), (1, 8))),
        "weight_blocks": gaussian(key_of[1], (FB, K, BLK, BLK), (K * BLK) ** -0.5, 0.3125, ((0, 8),)),
        "pattern": draw_pattern(jax.random.fold_in(key_of[4], 71), 0),
        "grad_out": gaussian(key_of[3], (TOKENS, F), 1.0, 6.0, ((0, 128), (1, 8))),
    }


def reference(tokens, weight_blocks, pattern, grad_out):
    count_rows = tokens.shape[0]
    token_rows = tokens.reshape(count_rows, RB, BLK)
    grad_cols = jnp.transpose(grad_out.reshape(count_rows, FB, BLK), (1, 0, 2))

    def column_step(carry, inputs):
        rows, weights, grad_block = inputs
        picked = jnp.take(token_rows, rows, axis=1).astype(jnp.float32)
        weights_wide = weights.astype(jnp.float32)
        grad_wide = grad_block.astype(jnp.float32)
        output_block = jnp.einsum('tkb,kbo->to', picked, weights_wide).astype(jnp.bfloat16)
        backward = jnp.einsum('to,kbo->tkb', grad_wide, weights_wide)
        carry = carry.at[:, rows].add(backward)
        weight_grad = jnp.einsum('tkb,to->kbo', picked, grad_wide)
        return (carry, (output_block, weight_grad))
    start = jnp.zeros((count_rows, RB, BLK), jnp.float32)
    summed, (outputs, weight_grads) = lax.scan(column_step, start, (pattern, weight_blocks, grad_cols))
    projected = jnp.transpose(outputs, (1, 0, 2)).reshape(count_rows, FB * BLK)
    grad_tokens = summed.reshape(count_rows, D).astype(jnp.bfloat16)
    grad_weight = (weight_grads / jnp.sqrt(jnp.float32(TOKENS))).reshape(FB, K, BLK * BLK)
    return (projected, grad_tokens, grad_weight)
```

```python
import jax
import jax.numpy as jnp
from jax import lax
from jax.sharding import Mesh
from jax.sharding import PartitionSpec as P

DP_SPLIT = (("z", 16), ("yh", 4), ("c", 2))
DP = tuple(name for name, _ in DP_SPLIT)


def reduce_over_dp(terms):
    rows, width = terms.shape
    pairs = terms.reshape(rows // 2, 2, width)
    mine = lax.axis_index("c")
    keep = lax.dynamic_index_in_dim(pairs, mine, axis=1, keepdims=False)
    send = lax.dynamic_index_in_dim(pairs, 1 - mine, axis=1, keepdims=False)
    halved = keep + lax.ppermute(send, "c", [(0, 1), (1, 0)])
    planes, lanes = DP_SPLIT[0][1], DP_SPLIT[1][1]
    across = halved.reshape(planes, lanes, width).transpose(1, 0, 2).reshape(lanes, planes * width)
    across = jnp.sum(lax.all_to_all(across, "yh", 0, 0, tiled=True), axis=0)
    along = lax.all_to_all(across.reshape(planes, width), "z", 0, 0, tiled=True)
    return jnp.sum(along, axis=0)


def on_device(tokens, weight_blocks, pattern, grad_out):
    count_rows = tokens.shape[0]
    columns, slots, block_size = (
        weight_blocks.shape[0],
        weight_blocks.shape[1],
        weight_blocks.shape[3],
    )
    whole = lax.all_gather(tokens, "fsdp", axis=1, tiled=True)
    width = whole.shape[1]
    row_blocks = width // block_size
    whole_rows = whole.reshape(count_rows, row_blocks, block_size)
    grad_cols = grad_out.reshape(count_rows, columns, block_size)
    row_ids = jnp.arange(row_blocks, dtype=jnp.int32)
    projected_sum = jnp.zeros((count_rows, columns, block_size), jnp.float32)
    partial_grads = jnp.zeros((count_rows, row_blocks, block_size), jnp.float32)
    slot_terms = []
    for slot in range(slots):
        selector = row_ids[:, None] == pattern[:, slot][None, :]
        picked_slot = jnp.einsum(
            "trb,rc->tcb",
            whole_rows,
            selector.astype(jnp.bfloat16),
            preferred_element_type=jnp.float32,
        ).astype(jnp.bfloat16)
        weight_slot = weight_blocks[:, slot]
        projected_sum = projected_sum + jnp.einsum(
            "tcb,cbo->tco", picked_slot, weight_slot, preferred_element_type=jnp.float32
        )
        backward_slot = jnp.einsum(
            "tco,cbo->tcb", grad_cols, weight_slot, preferred_element_type=jnp.float32
        )
        partial_grads = partial_grads + jnp.einsum(
            "tcb,rc->trb",
            backward_slot,
            selector.astype(jnp.float32),
            precision=lax.Precision.HIGHEST,
        )
        slot_terms.append(
            jnp.einsum("tcb,tco->bco", picked_slot, grad_cols, preferred_element_type=jnp.float32)
        )
    projected = projected_sum.astype(jnp.bfloat16).reshape(count_rows, columns * block_size)
    partial_grads = partial_grads.reshape(count_rows, width)
    grad_tokens = lax.psum_scatter(partial_grads, "fsdp", scatter_dimension=1, tiled=True).astype(
        jnp.bfloat16
    )
    scale_factor = 1.0 / jnp.sqrt(jnp.float32(count_rows * lax.axis_size(DP)))
    weight_terms = jnp.stack(slot_terms, axis=2).reshape(block_size, columns * slots * block_size)
    grad_weight = reduce_over_dp(weight_terms).reshape(columns, slots, block_size) * scale_factor
    return (projected, grad_tokens, grad_weight)


def solution(mesh):
    split = Mesh(
        mesh.devices.reshape(tuple(size for _, size in DP_SPLIT) + (mesh.shape["fsdp"],)),
        DP + ("fsdp",),
    )
    placed = (P(DP, "fsdp"), P("fsdp", None, None, None), P("fsdp", None), P(DP, "fsdp"))
    return jax.shard_map(
        on_device,
        mesh=split,
        in_specs=placed,
        out_specs=(P(DP, "fsdp"), P(DP, "fsdp"), P("fsdp", None, DP)),
        check_vma=False,
    )
```

```python
import jax
import jax.numpy as jnp
from jax import lax
from jax.sharding import Mesh
from jax.sharding import PartitionSpec as P

DP_SPLIT = (("z", 16), ("yh", 4), ("c", 2))
DP = tuple(name for name, _ in DP_SPLIT)
FSDP_SPLIT = (("yl", 2), ("x", 4))
FSDP = tuple(name for name, _ in FSDP_SPLIT)


def reduce_over_dp(terms):
    rows, width = terms.shape
    pairs = terms.reshape(rows // 2, 2, width)
    mine = lax.axis_index("c")
    keep = lax.dynamic_index_in_dim(pairs, mine, axis=1, keepdims=False)
    send = lax.dynamic_index_in_dim(pairs, 1 - mine, axis=1, keepdims=False)
    halved = keep + lax.ppermute(send, "c", [(0, 1), (1, 0)])
    planes, lanes = DP_SPLIT[0][1], DP_SPLIT[1][1]
    across = halved.reshape(planes, lanes, width).transpose(1, 0, 2).reshape(lanes, planes * width)
    across = jnp.sum(lax.all_to_all(across, "yh", 0, 0, tiled=True), axis=0)
    along = lax.all_to_all(across.reshape(planes, width), "z", 0, 0, tiled=True)
    return jnp.sum(along, axis=0)


def on_device(tokens, weight_blocks, pattern, grad_out):
    count_rows = tokens.shape[0]
    columns, slots, block_size = (
        weight_blocks.shape[0],
        weight_blocks.shape[1],
        weight_blocks.shape[3],
    )
    pair = lax.all_gather(tokens, "yl", axis=0, tiled=False)
    ring = lax.all_gather(pair, "x", axis=1, tiled=False)
    whole = ring.transpose(2, 0, 1, 3).reshape(count_rows, -1)
    width = whole.shape[1]
    row_blocks = width // block_size
    whole_rows = whole.reshape(count_rows, row_blocks, block_size)
    grad_cols = grad_out.reshape(count_rows, columns, block_size)
    row_ids = jnp.arange(row_blocks, dtype=jnp.int32)
    projected_sum = jnp.zeros((count_rows, columns, block_size), jnp.float32)
    partial_grads = jnp.zeros((count_rows, row_blocks, block_size), jnp.float32)
    slot_terms = []
    for slot in range(slots):
        selector = row_ids[:, None] == pattern[:, slot][None, :]
        picked_slot = jnp.einsum(
            "trb,rc->tcb",
            whole_rows,
            selector.astype(jnp.bfloat16),
            preferred_element_type=jnp.float32,
        ).astype(jnp.bfloat16)
        weight_slot = weight_blocks[:, slot]
        projected_sum = projected_sum + jnp.einsum(
            "tcb,cbo->tco", picked_slot, weight_slot, preferred_element_type=jnp.float32
        )
        backward_slot = jnp.einsum(
            "tco,cbo->tcb", grad_cols, weight_slot, preferred_element_type=jnp.float32
        )
        partial_grads = partial_grads + jnp.einsum(
            "tcb,rc->trb",
            backward_slot,
            selector.astype(jnp.float32),
            precision=lax.Precision.HIGHEST,
        )
        slot_terms.append(
            jnp.einsum("tcb,tco->bco", picked_slot, grad_cols, preferred_element_type=jnp.float32)
        )
    projected = projected_sum.astype(jnp.bfloat16).reshape(count_rows, columns * block_size)
    partial_grads = partial_grads.reshape(count_rows, width)
    grad_tokens = lax.psum_scatter(partial_grads, FSDP, scatter_dimension=1, tiled=True).astype(
        jnp.bfloat16
    )
    scale_factor = 1.0 / jnp.sqrt(jnp.float32(count_rows * lax.axis_size(DP)))
    weight_terms = jnp.stack(slot_terms, axis=2).reshape(block_size, columns * slots * block_size)
    grad_weight = reduce_over_dp(weight_terms).reshape(columns, slots, block_size) * scale_factor
    return (projected, grad_tokens, grad_weight)


def solution(mesh):
    split = Mesh(
        mesh.devices.reshape(tuple(size for _, size in DP_SPLIT + FSDP_SPLIT)),
        DP + FSDP,
    )
    placed = (P(DP, FSDP), P(FSDP, None, None, None), P(FSDP, None), P(DP, FSDP))
    return jax.shard_map(
        on_device,
        mesh=split,
        in_specs=placed,
        out_specs=(P(DP, FSDP), P(DP, FSDP), P(FSDP, None, DP)),
        check_vma=False,
    )
```

```python
import jax
import jax.numpy as jnp
from jax import lax
from jax.sharding import Mesh
from jax.sharding import PartitionSpec as P

DP_SPLIT = (("z", 16), ("yh", 4), ("c", 2))
DP = tuple(name for name, _ in DP_SPLIT)
FSDP_SPLIT = (("yl", 2), ("x", 4))
FSDP = tuple(name for name, _ in FSDP_SPLIT)


def reduce_over_dp(keep, send):
    rows, width = keep.shape
    halved = keep + lax.ppermute(send, "c", [(0, 1), (1, 0)])
    planes, lanes = DP_SPLIT[0][1], DP_SPLIT[1][1]
    across = halved.reshape(planes, lanes, width).transpose(1, 0, 2).reshape(lanes, planes * width)
    across = jnp.sum(lax.all_to_all(across, "yh", 0, 0, tiled=True), axis=0)
    along = lax.all_to_all(across.reshape(planes, width), "z", 0, 0, tiled=True)
    return jnp.sum(along, axis=0)


def on_device(tokens, weight_blocks, pattern, grad_out):
    count_rows = tokens.shape[0]
    columns, slots, block_size = (
        weight_blocks.shape[0],
        weight_blocks.shape[1],
        weight_blocks.shape[3],
    )
    pair = lax.all_gather(tokens, "yl", axis=0, tiled=False)
    ring = lax.all_gather(pair, "x", axis=1, tiled=False)
    whole = ring.transpose(2, 0, 1, 3).reshape(count_rows, -1)
    width = whole.shape[1]
    row_blocks = width // block_size
    whole_rows = whole.reshape(count_rows, row_blocks, block_size)
    grad_cols = grad_out.reshape(count_rows, columns, block_size)
    row_ids = jnp.arange(row_blocks, dtype=jnp.int32)
    projected_sum = jnp.zeros((count_rows, columns, block_size), jnp.float32)
    partial_grads = jnp.zeros((count_rows, row_blocks, block_size), jnp.float32)
    keep_terms, send_terms = [], []
    first_core = lax.axis_index("c") == 0
    for slot in range(slots):
        selector = row_ids[:, None] == pattern[:, slot][None, :]
        picked_slot = jnp.einsum(
            "trb,rc->tcb",
            whole_rows,
            selector.astype(jnp.bfloat16),
            preferred_element_type=jnp.float32,
        ).astype(jnp.bfloat16)
        weight_slot = weight_blocks[:, slot]
        projected_sum = projected_sum + jnp.einsum(
            "tcb,cbo->tco", picked_slot, weight_slot, preferred_element_type=jnp.float32
        )
        backward_slot = jnp.einsum(
            "tco,cbo->tcb", grad_cols, weight_slot, preferred_element_type=jnp.float32
        )
        partial_grads = partial_grads + jnp.einsum(
            "tcb,rc->trb",
            backward_slot,
            selector.astype(jnp.float32),
            precision=lax.Precision.HIGHEST,
        )
        even, odd = picked_slot[:, :, 0::2], picked_slot[:, :, 1::2]
        for terms, rows in ((keep_terms, jnp.where(first_core, even, odd)), (send_terms, jnp.where(first_core, odd, even))):
            terms.append(
                jnp.einsum("tcb,tco->bco", rows, grad_cols, preferred_element_type=jnp.float32)
            )
    projected = projected_sum.astype(jnp.bfloat16).reshape(count_rows, columns * block_size)
    partial_grads = partial_grads.reshape(count_rows, width)
    grad_tokens = lax.psum_scatter(partial_grads, FSDP, scatter_dimension=1, tiled=True).astype(
        jnp.bfloat16
    )
    scale_factor = 1.0 / jnp.sqrt(jnp.float32(count_rows * lax.axis_size(DP)))
    keep = jnp.stack(keep_terms, axis=2).reshape(block_size // 2, columns * slots * block_size)
    send = jnp.stack(send_terms, axis=2).reshape(block_size // 2, columns * slots * block_size)
    grad_weight = reduce_over_dp(keep, send).reshape(columns, slots, block_size) * scale_factor
    return (projected, grad_tokens, grad_weight)


def solution(mesh):
    split = Mesh(
        mesh.devices.reshape(tuple(size for _, size in DP_SPLIT + FSDP_SPLIT)),
        DP + FSDP,
    )
    placed = (P(DP, FSDP), P(FSDP, None, None, None), P(FSDP, None), P(DP, FSDP))
    return jax.shard_map(
        on_device,
        mesh=split,
        in_specs=placed,
        out_specs=(P(DP, FSDP), P(DP, FSDP), P(FSDP, None, DP)),
        check_vma=False,
    )
```

```python
import jax
import jax.numpy as jnp
from jax import lax
from jax.sharding import Mesh
from jax.sharding import PartitionSpec as P

DP_SPLIT = (("z", 16), ("yh", 4), ("c", 2))
DP = tuple(name for name, _ in DP_SPLIT)
FSDP_SPLIT = (("yl", 2), ("x", 4))
FSDP = tuple(name for name, _ in FSDP_SPLIT)


def reduce_over_dp(keep, send):
    rows, width = keep.shape
    halved = keep + lax.ppermute(send, "c", [(0, 1), (1, 0)])
    planes, lanes = DP_SPLIT[0][1], DP_SPLIT[1][1]
    across = halved.reshape(planes, lanes, width).transpose(1, 0, 2).reshape(lanes, planes * width)
    across = jnp.sum(lax.all_to_all(across, "yh", 0, 0, tiled=True), axis=0)
    along = lax.all_to_all(across.reshape(planes, width), "z", 0, 0, tiled=True)
    return jnp.sum(along, axis=0)


def on_device(tokens, weight_blocks, pattern, grad_out):
    count_rows = tokens.shape[0]
    columns, slots, block_size = (
        weight_blocks.shape[0],
        weight_blocks.shape[1],
        weight_blocks.shape[3],
    )
    pair = lax.all_gather(tokens, "yl", axis=0, tiled=False)
    ring = lax.all_gather(pair, "x", axis=1, tiled=False)
    whole = ring.transpose(2, 0, 1, 3).reshape(count_rows, -1)
    width = whole.shape[1]
    row_blocks = width // block_size
    whole_rows = whole.reshape(count_rows, row_blocks, block_size)
    grad_cols = grad_out.reshape(count_rows, columns, block_size)
    row_ids = jnp.arange(row_blocks, dtype=jnp.int32)
    projected_sum = jnp.zeros((count_rows, columns, block_size), jnp.float32)
    partial_grads = jnp.zeros((count_rows, row_blocks, block_size), jnp.float32)
    keep_terms, send_terms = [], []
    core = lax.axis_index("c")
    column_ids = jnp.arange(block_size, dtype=jnp.int32)[:, None]
    pair_ids = 2 * jnp.arange(block_size // 2, dtype=jnp.int32)[None, :]
    keep_cols = (column_ids == pair_ids + core).astype(jnp.bfloat16)
    send_cols = (column_ids == pair_ids + 1 - core).astype(jnp.bfloat16)
    for slot in range(slots):
        selector = row_ids[:, None] == pattern[:, slot][None, :]
        picked_slot = jnp.einsum(
            "trb,rc->tcb",
            whole_rows,
            selector.astype(jnp.bfloat16),
            preferred_element_type=jnp.float32,
        ).astype(jnp.bfloat16)
        weight_slot = weight_blocks[:, slot]
        projected_sum = projected_sum + jnp.einsum(
            "tcb,cbo->tco", picked_slot, weight_slot, preferred_element_type=jnp.float32
        )
        backward_slot = jnp.einsum(
            "tco,cbo->tcb", grad_cols, weight_slot, preferred_element_type=jnp.float32
        )
        partial_grads = partial_grads + jnp.einsum(
            "tcb,rc->trb",
            backward_slot,
            selector.astype(jnp.float32),
            precision=lax.Precision.HIGHEST,
        )
        for terms, cols in ((keep_terms, keep_cols), (send_terms, send_cols)):
            rows = jnp.einsum(
                "tcb,bm->tcm", picked_slot, cols, preferred_element_type=jnp.float32
            ).astype(jnp.bfloat16)
            terms.append(
                jnp.einsum("tcb,tco->bco", rows, grad_cols, preferred_element_type=jnp.float32)
            )
    projected = projected_sum.astype(jnp.bfloat16).reshape(count_rows, columns * block_size)
    partial_grads = partial_grads.reshape(count_rows, width)
    grad_tokens = lax.psum_scatter(partial_grads, FSDP, scatter_dimension=1, tiled=True).astype(
        jnp.bfloat16
    )
    scale_factor = 1.0 / jnp.sqrt(jnp.float32(count_rows * lax.axis_size(DP)))
    keep = jnp.stack(keep_terms, axis=2).reshape(block_size // 2, columns * slots * block_size)
    send = jnp.stack(send_terms, axis=2).reshape(block_size // 2, columns * slots * block_size)
    grad_weight = reduce_over_dp(keep, send).reshape(columns, slots, block_size) * scale_factor
    return (projected, grad_tokens, grad_weight)


def solution(mesh):
    split = Mesh(
        mesh.devices.reshape(tuple(size for _, size in DP_SPLIT + FSDP_SPLIT)),
        DP + FSDP,
    )
    placed = (P(DP, FSDP), P(FSDP, None, None, None), P(FSDP, None), P(DP, FSDP))
    return jax.shard_map(
        on_device,
        mesh=split,
        in_specs=placed,
        out_specs=(P(DP, FSDP), P(DP, FSDP), P(FSDP, None, DP)),
        check_vma=False,
    )
```

```python
import jax
import jax.numpy as jnp
from jax import lax
from jax.sharding import Mesh
from jax.sharding import PartitionSpec as P

DP_SPLIT = (("z", 16), ("yh", 4), ("c", 2))
DP = tuple(name for name, _ in DP_SPLIT)
FSDP_SPLIT = (("yl", 2), ("x", 4))
FSDP = tuple(name for name, _ in FSDP_SPLIT)


def reduce_over_dp(terms):
    rows, width = terms.shape
    pairs = terms.reshape(rows // 2, 2, width)
    mine = lax.axis_index("c")
    first = mine == 0
    keep = jnp.where(first, pairs[:, 0], pairs[:, 1])
    send = jnp.where(first, pairs[:, 1], pairs[:, 0])
    halved = keep + lax.ppermute(send, "c", [(0, 1), (1, 0)])
    planes, lanes = DP_SPLIT[0][1], DP_SPLIT[1][1]
    across = halved.reshape(planes, lanes, width).transpose(1, 0, 2).reshape(lanes, planes * width)
    across = jnp.sum(lax.all_to_all(across, "yh", 0, 0, tiled=True), axis=0)
    along = lax.all_to_all(across.reshape(planes, width), "z", 0, 0, tiled=True)
    return jnp.sum(along, axis=0)


def on_device(tokens, weight_blocks, pattern, grad_out):
    count_rows = tokens.shape[0]
    columns, slots, block_size = (
        weight_blocks.shape[0],
        weight_blocks.shape[1],
        weight_blocks.shape[3],
    )
    pair = lax.all_gather(tokens, "yl", axis=0, tiled=False)
    ring = lax.all_gather(pair, "x", axis=1, tiled=False)
    whole = ring.transpose(2, 0, 1, 3).reshape(count_rows, -1)
    width = whole.shape[1]
    row_blocks = width // block_size
    whole_rows = whole.reshape(count_rows, row_blocks, block_size)
    grad_cols = grad_out.reshape(count_rows, columns, block_size)
    row_ids = jnp.arange(row_blocks, dtype=jnp.int32)
    projected_sum = jnp.zeros((count_rows, columns, block_size), jnp.float32)
    partial_grads = jnp.zeros((count_rows, row_blocks, block_size), jnp.float32)
    slot_terms = []
    for slot in range(slots):
        selector = row_ids[:, None] == pattern[:, slot][None, :]
        picked_slot = jnp.einsum(
            "trb,rc->tcb",
            whole_rows,
            selector.astype(jnp.bfloat16),
            preferred_element_type=jnp.float32,
        ).astype(jnp.bfloat16)
        weight_slot = weight_blocks[:, slot]
        projected_sum = projected_sum + jnp.einsum(
            "tcb,cbo->tco", picked_slot, weight_slot, preferred_element_type=jnp.float32
        )
        backward_slot = jnp.einsum(
            "tco,cbo->tcb", grad_cols, weight_slot, preferred_element_type=jnp.float32
        )
        partial_grads = partial_grads + jnp.einsum(
            "tcb,rc->trb",
            backward_slot,
            selector.astype(jnp.float32),
            precision=lax.Precision.HIGHEST,
        )
        slot_terms.append(
            jnp.einsum("tcb,tco->bco", picked_slot, grad_cols, preferred_element_type=jnp.float32)
        )
    projected = projected_sum.astype(jnp.bfloat16).reshape(count_rows, columns * block_size)
    partial_grads = partial_grads.reshape(count_rows, width)
    grad_tokens = lax.psum_scatter(partial_grads, FSDP, scatter_dimension=1, tiled=True).astype(
        jnp.bfloat16
    )
    scale_factor = 1.0 / jnp.sqrt(jnp.float32(count_rows * lax.axis_size(DP)))
    weight_terms = jnp.stack(slot_terms, axis=2).reshape(block_size, columns * slots * block_size)
    grad_weight = reduce_over_dp(weight_terms).reshape(columns, slots, block_size) * scale_factor
    return (projected, grad_tokens, grad_weight)


def solution(mesh):
    split = Mesh(
        mesh.devices.reshape(tuple(size for _, size in DP_SPLIT + FSDP_SPLIT)),
        DP + FSDP,
    )
    placed = (P(DP, FSDP), P(FSDP, None, None, None), P(FSDP, None), P(DP, FSDP))
    return jax.shard_map(
        on_device,
        mesh=split,
        in_specs=placed,
        out_specs=(P(DP, FSDP), P(DP, FSDP), P(FSDP, None, DP)),
        check_vma=False,
    )
```
